256 devices in a mesh: dp: 4 (over y_lo, core), row: 8 (over y_hi, x), col: 8 (over z).
Axes of the slice: x: 4, y: 4 (y_hi: 2, y_lo: 2; y = y_hi * 2 + y_lo), z: 8, core: 2. Of those that a mesh axis runs over, the one named last changes fastest.
Arguments:
- tokens: bfloat16 [3072, 4096], P('dp', ('row', 'col')), may hold values from -6 to 6
- cotangent: bfloat16 [3072, 4096], P('dp', ('row', 'col')), may hold values from -4 to 4
- gate_weight: bfloat16 [4096, 14336], P('row', 'col'), may hold values from -0.09375 to 0.09375
- up_weight: bfloat16 [4096, 14336], P('row', 'col'), may hold values from -0.09375 to 0.09375
- down_weight: bfloat16 [14336, 4096], P('col', 'row'), may hold values from -0.046875 to 0.046875
Outputs:
- layer_out: bfloat16 [3072, 4096], P(('dp', 'col'), 'row')
- input_grad: bfloat16 [3072, 4096], P(('dp', 'col'), 'row')
- gate_wgrad: bfloat16 [4096, 14336], P('row', 'col')
- up_wgrad: bfloat16 [4096, 14336], P('row', 'col')
- down_wgrad: bfloat16 [14336, 4096], P('col', 'row')
The draws below stay inside these ranges and needn't reach their ends.
All inputs are finite; a program needn't handle non-finite values.
Results may differ from the reference program's by a relative error of at most 0.034.
Values may be sent and summed in bfloat16 or wider, within the bound.
No kernel may reach another device: no remote copies, remote signals or barrier semaphores. Data moves between devices by JAX's collectives and lax.ppermute only.
A program may use at most 128 MiB of HBM per device.

```python
import jax
import jax.numpy as jnp

D = 4096
FF = 14336
TOK_GRP = 768
TOKENS = 3072
N_DP = 4
N_ROW = 8
N_COL = 8


def steps_of(own_key, shape, cuts, low, largest):
    def one(position, blocks):
        steps = jax.random.uniform(jax.random.fold_in(jax.random.fold_in(own_key, 6), position), (blocks,), jnp.float32, low / len(cuts), largest / len(cuts))
        return jnp.repeat(jnp.exp(steps), shape[position] // blocks).reshape((-1,) + (1,) * (len(shape) - position - 1))

    loudness = one(*cuts[0])
    for cut in cuts[1:]:
        loudness = loudness * one(*cut)
    return loudness


def gaussian(key, extent, spread, limit, split=(), kind=jnp.bfloat16):
    loudness = steps_of(key, extent, split, -0.22, 0.18) if split else 1.0
    entries = jax.random.normal(key, extent, jnp.float32) * spread * loudness
    return jnp.minimum(jnp.maximum(entries, -limit), limit).astype(kind)


def setup_inputs(seed: int = 0) -> dict:
    streams_of = jax.random.split(jax.random.key(seed), 6)
    tokens = gaussian(streams_of[0], (TOKENS, D), 1.0, 6.0, ((0, 4), (1, 64)))
    cotangent = gaussian(streams_of[1], (TOKENS, D), 0.25, 4.0, ((0, 4), (1, 64)))
    gate_weight = gaussian(streams_of[2], (D, FF), D ** -0.5, 0.09375, ((0, 8), (1, 8)))
    up_weight = gaussian(streams_of[3], (D, FF), D ** -0.5, 0.09375, ((0, 8), (1, 8)))
    down_weight = gaussian(streams_of[4], (FF, D), FF ** -0.5, 0.046875, ((0, 8), (1, 8)))
    return {"tokens": tokens, "cotangent": cotangent, "gate_weight": gate_weight, "up_weight": up_weight, "down_weight": down_weight}


def blocked(left, right, parts):
    width = left.shape[1] // parts
    total = jnp.zeros((left.shape[0], right.shape[1]), jnp.float32)
    for block in range(parts):
        term = jnp.dot(left[:, block * width:(block + 1) * width], right[block * width:(block + 1) * width],
                       preferred_element_type=jnp.float32)
        total = total + term.astype(jnp.bfloat16).astype(jnp.float32)
    return total


def input_blocked(gate_grad, up_grad, gate_weight, up_weight, parts):
    width = gate_grad.shape[1] // parts
    total = jnp.zeros((gate_grad.shape[0], gate_weight.shape[0]), jnp.float32)
    for block in range(parts):
        lo = block * width
        hi = lo + width
        term = (jnp.dot(gate_grad[:, lo:hi], gate_weight[:, lo:hi].T, preferred_element_type=jnp.float32)
                + jnp.dot(up_grad[:, lo:hi], up_weight[:, lo:hi].T, preferred_element_type=jnp.float32))
        total = total + term.astype(jnp.bfloat16).astype(jnp.float32)
    return total


def group_pass(x, dy, gate_weight, up_weight, down_weight):
    f32 = jnp.float32
    gate = blocked(x, gate_weight, N_ROW)
    up = blocked(x, up_weight, N_ROW)
    sigma = jax.nn.sigmoid(gate)
    silu_gate = gate * sigma
    hidden = (silu_gate * up).astype(jnp.bfloat16)
    layer_out = blocked(hidden, down_weight, N_COL).astype(jnp.bfloat16)
    hidden_grad = blocked(dy, down_weight.T, N_ROW)
    gate_grad = (hidden_grad * up * sigma * (1.0 + gate * (1.0 - sigma))).astype(jnp.bfloat16)
    up_grad = (hidden_grad * silu_gate).astype(jnp.bfloat16)
    input_grad = input_blocked(gate_grad, up_grad, gate_weight, up_weight, N_COL).astype(jnp.bfloat16)
    down_part = jnp.dot(hidden.T, dy, preferred_element_type=f32).astype(jnp.bfloat16)
    gate_part = jnp.dot(x.T, gate_grad, preferred_element_type=f32).astype(jnp.bfloat16)
    up_part = jnp.dot(x.T, up_grad, preferred_element_type=f32).astype(jnp.bfloat16)
    return layer_out, input_grad, gate_part, up_part, down_part


def reference(tokens, cotangent, gate_weight, up_weight, down_weight):
    outputs = []
    in_grads = []
    gate_total = jnp.zeros((D, FF), jnp.float32)
    up_total = jnp.zeros((D, FF), jnp.float32)
    down_total = jnp.zeros((FF, D), jnp.float32)
    for group in range(N_DP):
        x = tokens[group * TOK_GRP:(group + 1) * TOK_GRP]
        dy = cotangent[group * TOK_GRP:(group + 1) * TOK_GRP]
        layer_out, input_grad, gate_part, up_part, down_part = group_pass(x, dy, gate_weight, up_weight, down_weight)
        outputs.append(layer_out)
        in_grads.append(input_grad)
        gate_total = gate_total + gate_part.astype(jnp.float32)
        up_total = up_total + up_part.astype(jnp.float32)
        down_total = down_total + down_part.astype(jnp.float32)
    return (jnp.concatenate(outputs, axis=0), jnp.concatenate(in_grads, axis=0),
            gate_total.astype(jnp.bfloat16), up_total.astype(jnp.bfloat16), down_total.astype(jnp.bfloat16))
```

```python
import jax
import jax.numpy as jnp
from jax import lax
from jax.sharding import PartitionSpec as P

F32 = jnp.float32
BF16 = jnp.bfloat16


def contract_rows(left, right):
    return lax.dot_general(
        left, right, (((0,), (0,)), ((), ())), preferred_element_type=F32
    )


def contract_cols(left, right):
    return lax.dot_general(
        left, right, (((1,), (1,)), ((), ())), preferred_element_type=F32
    )


def shift_pairs(n, s):
    return [(i, (i + s) % n) for i in range(n)]


def gather_by_shifts(x, name, n, axis):
    me = lax.axis_index(name)
    blocks = [x]
    for t in range(1, n):
        blocks.append(lax.ppermute(x, name, shift_pairs(n, n - t)))
    doubled = jnp.concatenate(blocks + blocks, axis=axis)
    width = x.shape[axis]
    return lax.dynamic_slice_in_dim(doubled, (n - me) * width, n * width, axis=axis)


def scatter_sum_by_shifts(p, name, n, axis):
    me = lax.axis_index(name)
    width = p.shape[axis] // n
    acc = lax.dynamic_slice_in_dim(p, me * width, width, axis=axis).astype(F32)
    for s in range(1, n):
        block = lax.dynamic_slice_in_dim(p, ((me + s) % n) * width, width, axis=axis)
        acc = acc + lax.ppermute(block, name, shift_pairs(n, s)).astype(F32)
    return acc


def dp_allreduce(g):
    name = "dp"
    d = lax.axis_index(name)
    core = d % 2
    chip = d // 2
    to_core = [(i, i ^ 1) for i in range(4)]
    to_chip = [(i, i ^ 2) for i in range(4)]
    half = g.shape[0] // 2
    quarter = half // 2
    keep = lax.dynamic_slice_in_dim(g, core * half, half, 0)
    give = lax.dynamic_slice_in_dim(g, (1 - core) * half, half, 0)
    s1 = (keep.astype(F32) + lax.ppermute(give, name, to_core).astype(F32)).astype(BF16)
    keep2 = lax.dynamic_slice_in_dim(s1, chip * quarter, quarter, 0)
    give2 = lax.dynamic_slice_in_dim(s1, (1 - chip) * quarter, quarter, 0)
    s2 = (keep2.astype(F32) + lax.ppermute(give2, name, to_chip).astype(F32)).astype(BF16)
    other2 = lax.ppermute(s2, name, to_chip)
    mine_half = jnp.where(chip == 0, jnp.concatenate([s2, other2], 0), jnp.concatenate([other2, s2], 0))
    other_half = lax.ppermute(mine_half, name, to_core)
    return jnp.where(core == 0, jnp.concatenate([mine_half, other_half], 0),
                     jnp.concatenate([other_half, mine_half], 0))


def local(tokens, cotangent, gate_weight, up_weight, down_weight):
    n_col = 8
    feat = tokens.shape[1]
    both = gather_by_shifts(jnp.concatenate([tokens, cotangent], axis=1), "col", n_col, 0 + 1)
    both = both.reshape(both.shape[0], n_col, 2, feat)
    whole_x = both[:, :, 0, :].reshape(both.shape[0], n_col * feat)
    whole_dy = both[:, :, 1, :].reshape(both.shape[0], n_col * feat)
    width = gate_weight.shape[1]
    stacked = lax.psum_scatter(
        jnp.concatenate(
            [
                jnp.dot(whole_x, gate_weight, preferred_element_type=F32),
                jnp.dot(whole_x, up_weight, preferred_element_type=F32),
            ],
            axis=1,
        ).astype(BF16),
        "row",
        scatter_dimension=0,
        tiled=True,
    ).astype(F32)
    gate = stacked[:, :width]
    up = stacked[:, width:]
    sigma = jax.nn.sigmoid(gate)
    silu_gate = gate * sigma
    hidden = (silu_gate * up).astype(BF16)
    hidden_all = lax.all_gather(hidden, "row", axis=0, tiled=True)
    out_terms = jnp.dot(hidden_all, down_weight, preferred_element_type=F32)
    layer_out = scatter_sum_by_shifts(out_terms.astype(BF16), "col", n_col, 0).astype(BF16)
    down_part = contract_rows(hidden_all, whole_dy).astype(BF16)
    down_wgrad = dp_allreduce(down_part)
    hidden_grad = lax.psum_scatter(
        contract_cols(whole_dy, down_weight).astype(BF16),
        "row",
        scatter_dimension=0,
        tiled=True,
    ).astype(F32)
    gate_grad = (hidden_grad * up * sigma * (1.0 + gate * (1.0 - sigma))).astype(BF16)
    up_grad = (hidden_grad * silu_gate).astype(BF16)
    gate_all = lax.all_gather(gate_grad, "row", axis=0, tiled=True)
    gate_part = contract_rows(whole_x, gate_all).astype(BF16)
    gate_wgrad = dp_allreduce(gate_part)
    up_all = lax.all_gather(up_grad, "row", axis=0, tiled=True)
    up_part = contract_rows(whole_x, up_all).astype(BF16)
    up_wgrad = dp_allreduce(up_part)
    input_terms = (contract_cols(gate_all, gate_weight) + contract_cols(up_all, up_weight)).astype(BF16)
    input_grad = scatter_sum_by_shifts(input_terms, "col", n_col, 0).astype(BF16)
    return (layer_out, input_grad, gate_wgrad, up_wgrad, down_wgrad)


def solution(mesh):
    in_specs = (
        P("dp", ("row", "col")),
        P("dp", ("row", "col")),
        P("row", "col"),
        P("row", "col"),
        P("col", "row"),
    )
    out_specs = (
        P(("dp", "col"), "row"),
        P(("dp", "col"), "row"),
        P("row", "col"),
        P("row", "col"),
        P("col", "row"),
    )
    return jax.shard_map(local, mesh=mesh, in_specs=in_specs, out_specs=out_specs, check_vma=False)
```

```python
import jax
import jax.numpy as jnp
from jax import lax
from jax.sharding import PartitionSpec as P

F32 = jnp.float32
BF16 = jnp.bfloat16


def contract_rows(left, right):
    return lax.dot_general(
        left, right, (((0,), (0,)), ((), ())), preferred_element_type=F32
    )


def contract_cols(left, right):
    return lax.dot_general(
        left, right, (((1,), (1,)), ((), ())), preferred_element_type=F32
    )


def shift_pairs(n, s):
    return [(i, (i + s) % n) for i in range(n)]


def gather_by_shifts(x, name, n, axis):
    me = lax.axis_index(name)
    blocks = [x]
    for t in range(1, n):
        blocks.append(lax.ppermute(x, name, shift_pairs(n, n - t)))
    doubled = jnp.concatenate(blocks + blocks, axis=axis)
    width = x.shape[axis]
    return lax.dynamic_slice_in_dim(doubled, (n - me) * width, n * width, axis=axis)


def scatter_sum_by_shifts(p, name, n, axis):
    me = lax.axis_index(name)
    width = p.shape[axis] // n
    acc = lax.dynamic_slice_in_dim(p, me * width, width, axis=axis).astype(F32)
    for s in range(1, n):
        block = lax.dynamic_slice_in_dim(p, ((me + s) % n) * width, width, axis=axis)
        acc = acc + lax.ppermute(block, name, shift_pairs(n, s)).astype(F32)
    return acc


def dp_allreduce(g):
    name = "dp"
    d = lax.axis_index(name)
    core = d % 2
    chip = d // 2
    to_core = [(i, i ^ 1) for i in range(4)]
    to_chip = [(i, i ^ 2) for i in range(4)]
    half = g.shape[0] // 2
    quarter = half // 2
    keep = lax.dynamic_slice_in_dim(g, core * half, half, 0)
    give = lax.dynamic_slice_in_dim(g, (1 - core) * half, half, 0)
    s1 = (keep.astype(F32) + lax.ppermute(give, name, to_core).astype(F32)).astype(BF16)
    keep2 = lax.dynamic_slice_in_dim(s1, chip * quarter, quarter, 0)
    give2 = lax.dynamic_slice_in_dim(s1, (1 - chip) * quarter, quarter, 0)
    s2 = (keep2.astype(F32) + lax.ppermute(give2, name, to_chip).astype(F32)).astype(BF16)
    other2 = lax.ppermute(s2, name, to_chip)
    mine_half = jnp.where(chip == 0, jnp.concatenate([s2, other2], 0), jnp.concatenate([other2, s2], 0))
    other_half = lax.ppermute(mine_half, name, to_core)
    return jnp.where(core == 0, jnp.concatenate([mine_half, other_half], 0),
                     jnp.concatenate([other_half, mine_half], 0))


def local(tokens, cotangent, gate_weight, up_weight, down_weight):
    n_col = 8
    n_row = 8
    whole_xt = lax.all_gather(tokens.T, "col", axis=0, tiled=True)
    whole_dy = gather_by_shifts(cotangent, "col", n_col, 1)
    width = gate_weight.shape[1]
    stacked = lax.psum_scatter(
        jnp.concatenate(
            [
                contract_rows(whole_xt, gate_weight),
                contract_rows(whole_xt, up_weight),
            ],
            axis=1,
        ).astype(BF16),
        "row",
        scatter_dimension=0,
        tiled=True,
    ).astype(F32)
    hidden_grad = scatter_sum_by_shifts(
        contract_cols(whole_dy, down_weight).astype(BF16), "row", n_row, 0)
    gate = stacked[:, :width]
    up = stacked[:, width:]
    sigma = jax.nn.sigmoid(gate)
    silu_gate = gate * sigma
    hidden = (silu_gate * up).astype(BF16)
    hidden_all = lax.all_gather(hidden, "row", axis=0, tiled=True)
    out_terms = jnp.dot(hidden_all, down_weight, preferred_element_type=F32)
    layer_out = scatter_sum_by_shifts(out_terms.astype(BF16), "col", n_col, 0).astype(BF16)
    down_part = contract_rows(hidden_all, whole_dy).astype(BF16)
    down_wgrad = dp_allreduce(down_part)
    gate_grad = (hidden_grad * up * sigma * (1.0 + gate * (1.0 - sigma))).astype(BF16)
    up_grad = (hidden_grad * silu_gate).astype(BF16)
    up_all = gather_by_shifts(up_grad, "row", n_row, 0)
    down_part, gate_grad = lax.optimization_barrier((down_part, gate_grad))
    gate_all = lax.all_gather(gate_grad, "row", axis=0, tiled=True)
    up_part = jnp.dot(whole_xt, up_all, preferred_element_type=F32).astype(BF16)
    up_wgrad = dp_allreduce(up_part)
    gate_part = jnp.dot(whole_xt, gate_all, preferred_element_type=F32).astype(BF16)
    gate_wgrad = dp_allreduce(gate_part)
    input_terms = (contract_cols(gate_all, gate_weight) + contract_cols(up_all, up_weight)).astype(BF16)
    input_grad = scatter_sum_by_shifts(input_terms, "col", n_col, 0).astype(BF16)
    return (layer_out, input_grad, gate_wgrad, up_wgrad, down_wgrad)


def solution(mesh):
    in_specs = (
        P("dp", ("row", "col")),
        P("dp", ("row", "col")),
        P("row", "col"),
        P("row", "col"),
        P("col", "row"),
    )
    out_specs = (
        P(("dp", "col"), "row"),
        P(("dp", "col"), "row"),
        P("row", "col"),
        P("row", "col"),
        P("col", "row"),
    )
    return jax.shard_map(local, mesh=mesh, in_specs=in_specs, out_specs=out_specs, check_vma=False)
```

```python
import jax
import jax.numpy as jnp
from jax import lax
from jax.sharding import PartitionSpec as P

F32 = jnp.float32
BF16 = jnp.bfloat16


def contract_rows(left, right):
    return lax.dot_general(
        left, right, (((0,), (0,)), ((), ())), preferred_element_type=F32
    )


def contract_cols(left, right):
    return lax.dot_general(
        left, right, (((1,), (1,)), ((), ())), preferred_element_type=F32
    )


def shift_pairs(n, s):
    return [(i, (i + s) % n) for i in range(n)]


def gather_by_shifts(x, name, n, axis):
    me = lax.axis_index(name)
    blocks = [x]
    for t in range(1, n):
        blocks.append(lax.ppermute(x, name, shift_pairs(n, n - t)))
    doubled = jnp.concatenate(blocks + blocks, axis=axis)
    width = x.shape[axis]
    return lax.dynamic_slice_in_dim(doubled, (n - me) * width, n * width, axis=axis)


def scatter_sum_by_shifts(p, name, n, axis):
    me = lax.axis_index(name)
    width = p.shape[axis] // n
    acc = lax.dynamic_slice_in_dim(p, me * width, width, axis=axis).astype(F32)
    for s in range(1, n):
        block = lax.dynamic_slice_in_dim(p, ((me + s) % n) * width, width, axis=axis)
        acc = acc + lax.ppermute(block, name, shift_pairs(n, s)).astype(F32)
    return acc


def dp_allreduce(g):
    name = "dp"
    d = lax.axis_index(name)
    core = d % 2
    chip = d // 2
    to_core = [(i, i ^ 1) for i in range(4)]
    to_chip = [(i, i ^ 2) for i in range(4)]
    half = g.shape[0] // 2
    quarter = half // 2
    keep = lax.dynamic_slice_in_dim(g, core * half, half, 0)
    give = lax.dynamic_slice_in_dim(g, (1 - core) * half, half, 0)
    s1 = (keep.astype(F32) + lax.ppermute(give, name, to_core).astype(F32)).astype(BF16)
    keep2 = lax.dynamic_slice_in_dim(s1, chip * quarter, quarter, 0)
    give2 = lax.dynamic_slice_in_dim(s1, (1 - chip) * quarter, quarter, 0)
    s2 = (keep2.astype(F32) + lax.ppermute(give2, name, to_chip).astype(F32)).astype(BF16)
    other2 = lax.ppermute(s2, name, to_chip)
    mine_half = jnp.where(chip == 0, jnp.concatenate([s2, other2], 0), jnp.concatenate([other2, s2], 0))
    other_half = lax.ppermute(mine_half, name, to_core)
    return jnp.where(core == 0, jnp.concatenate([mine_half, other_half], 0),
                     jnp.concatenate([other_half, mine_half], 0))


def local(tokens, cotangent, gate_weight, up_weight, down_weight):
    n_col = 8
    n_row = 8
    whole_xt = lax.all_gather(tokens.T, "col", axis=0, tiled=True)
    whole_dy = gather_by_shifts(cotangent, "col", n_col, 1)
    gate = lax.psum_scatter(
        contract_rows(whole_xt, gate_weight).astype(BF16), "row", scatter_dimension=0, tiled=True
    ).astype(F32)
    up = scatter_sum_by_shifts(contract_rows(whole_xt, up_weight).astype(BF16), "row", n_row, 0)
    hidden_grad = scatter_sum_by_shifts(
        contract_cols(whole_dy, down_weight).astype(BF16), "row", n_row, 0)
    sigma = jax.nn.sigmoid(gate)
    silu_gate = gate * sigma
    hidden = (silu_gate * up).astype(BF16)
    hidden_all = lax.all_gather(hidden, "row", axis=0, tiled=True)
    out_terms = jnp.dot(hidden_all, down_weight, preferred_element_type=F32)
    layer_out = lax.psum_scatter(out_terms.astype(BF16), "col", scatter_dimension=0, tiled=True)
    down_part = contract_rows(hidden_all, whole_dy).astype(BF16)
    down_wgrad = dp_allreduce(down_part)
    gate_grad = (hidden_grad * up * sigma * (1.0 + gate * (1.0 - sigma))).astype(BF16)
    up_grad = (hidden_grad * silu_gate).astype(BF16)
    gate_all = gather_by_shifts(gate_grad, "row", n_row, 0)
    up_all = gather_by_shifts(up_grad, "row", n_row, 0)
    gate_part = jnp.dot(whole_xt, gate_all, preferred_element_type=F32).astype(BF16)
    gate_wgrad = dp_allreduce(gate_part)
    up_part = jnp.dot(whole_xt, up_all, preferred_element_type=F32).astype(BF16)
    up_wgrad = dp_allreduce(up_part)
    input_terms = (contract_cols(gate_all, gate_weight) + contract_cols(up_all, up_weight)).astype(BF16)
    input_grad = scatter_sum_by_shifts(input_terms, "col", n_col, 0).astype(BF16)
    return (layer_out, input_grad, gate_wgrad, up_wgrad, down_wgrad)


def solution(mesh):
    in_specs = (
        P("dp", ("row", "col")),
        P("dp", ("row", "col")),
        P("row", "col"),
        P("row", "col"),
        P("col", "row"),
    )
    out_specs = (
        P(("dp", "col"), "row"),
        P(("dp", "col"), "row"),
        P("row", "col"),
        P("row", "col"),
        P("col", "row"),
    )
    return jax.shard_map(local, mesh=mesh, in_specs=in_specs, out_specs=out_specs, check_vma=False)
```

```python
import jax
import jax.numpy as jnp
from jax import lax
from jax.sharding import PartitionSpec as P

F32 = jnp.float32
BF16 = jnp.bfloat16


def contract_rows(left, right):
    return lax.dot_general(
        left, right, (((0,), (0,)), ((), ())), preferred_element_type=F32
    )


def contract_cols(left, right):
    return lax.dot_general(
        left, right, (((1,), (1,)), ((), ())), preferred_element_type=F32
    )


def shift_pairs(n, s):
    return [(i, (i + s) % n) for i in range(n)]


def gather_by_shifts(x, name, n, axis):
    me = lax.axis_index(name)
    blocks = [x]
    for t in range(1, n):
        blocks.append(lax.ppermute(x, name, shift_pairs(n, n - t)))
    doubled = jnp.concatenate(blocks + blocks, axis=axis)
    width = x.shape[axis]
    return lax.dynamic_slice_in_dim(doubled, (n - me) * width, n * width, axis=axis)


def scatter_sum_by_shifts(p, name, n, axis):
    me = lax.axis_index(name)
    width = p.shape[axis] // n
    acc = lax.dynamic_slice_in_dim(p, me * width, width, axis=axis).astype(F32)
    for s in range(1, n):
        block = lax.dynamic_slice_in_dim(p, ((me + s) % n) * width, width, axis=axis)
        acc = acc + lax.ppermute(block, name, shift_pairs(n, s)).astype(F32)
    return acc


def dp_allreduce(g):
    name = "dp"
    d = lax.axis_index(name)
    core = d % 2
    chip = d // 2
    to_core = [(i, i ^ 1) for i in range(4)]
    to_chip = [(i, i ^ 2) for i in range(4)]
    half = g.shape[0] // 2
    quarter = half // 2
    keep = lax.dynamic_slice_in_dim(g, core * half, half, 0)
    give = lax.dynamic_slice_in_dim(g, (1 - core) * half, half, 0)
    s1 = (keep.astype(F32) + lax.ppermute(give, name, to_core).astype(F32)).astype(BF16)
    keep2 = lax.dynamic_slice_in_dim(s1, chip * quarter, quarter, 0)
    give2 = lax.dynamic_slice_in_dim(s1, (1 - chip) * quarter, quarter, 0)
    s2 = (keep2.astype(F32) + lax.ppermute(give2, name, to_chip).astype(F32)).astype(BF16)
    other2 = lax.ppermute(s2, name, to_chip)
    mine_half = jnp.where(chip == 0, jnp.concatenate([s2, other2], 0), jnp.concatenate([other2, s2], 0))
    other_half = lax.ppermute(mine_half, name, to_core)
    return jnp.where(core == 0, jnp.concatenate([mine_half, other_half], 0),
                     jnp.concatenate([other_half, mine_half], 0))


def row_scatter_sum(p):
    n_x = 4
    rows, cols = p.shape
    blk = rows // (2 * n_x)
    s1 = scatter_sum_by_shifts(p.reshape(2, n_x * blk, cols), "rx", n_x, 1).astype(BF16)
    h = lax.axis_index("rh")
    keep = lax.dynamic_index_in_dim(s1, h, 0, keepdims=False)
    give = lax.dynamic_index_in_dim(s1, 1 - h, 0, keepdims=False)
    return keep.astype(F32) + lax.ppermute(give, "rh", [(0, 1), (1, 0)]).astype(F32)


def row_gather(v):
    n_x = 4
    h = lax.axis_index("rh")
    other = lax.ppermute(v, "rh", [(0, 1), (1, 0)])
    pair = jnp.where(h == 0, jnp.stack([v, other]), jnp.stack([other, v]))
    got = gather_by_shifts(pair, "rx", n_x, 1)
    return got.reshape(2 * n_x * v.shape[0], v.shape[1])


def local(tokens, cotangent, gate_weight, up_weight, down_weight):
    n_col = 8
    row = ("rh", "rx")
    whole_xt = lax.all_gather(tokens.T, "col", axis=0, tiled=True)
    whole_dy = gather_by_shifts(cotangent, "col", n_col, 1)
    gate = lax.psum_scatter(
        contract_rows(whole_xt, gate_weight).astype(BF16), row, scatter_dimension=0, tiled=True
    ).astype(F32)
    up = row_scatter_sum(contract_rows(whole_xt, up_weight).astype(BF16))
    hidden_grad = row_scatter_sum(contract_cols(whole_dy, down_weight).astype(BF16))
    sigma = jax.nn.sigmoid(gate)
    silu_gate = gate * sigma
    hidden = (silu_gate * up).astype(BF16)
    hidden_all = lax.all_gather(hidden, row, axis=0, tiled=True)
    out_terms = jnp.dot(hidden_all, down_weight, preferred_element_type=F32)
    layer_out = lax.psum_scatter(out_terms.astype(BF16), "col", scatter_dimension=0, tiled=True)
    down_part = contract_rows(hidden_all, whole_dy).astype(BF16)
    down_wgrad = dp_allreduce(down_part)
    gate_grad = (hidden_grad * up * sigma * (1.0 + gate * (1.0 - sigma))).astype(BF16)
    up_grad = (hidden_grad * silu_gate).astype(BF16)
    gate_all = row_gather(gate_grad)
    up_all = row_gather(up_grad)
    gate_part = jnp.dot(whole_xt, gate_all, preferred_element_type=F32).astype(BF16)
    gate_wgrad = dp_allreduce(gate_part)
    up_part = jnp.dot(whole_xt, up_all, preferred_element_type=F32).astype(BF16)
    up_wgrad = dp_allreduce(up_part)
    input_terms = (contract_cols(gate_all, gate_weight) + contract_cols(up_all, up_weight)).astype(BF16)
    input_grad = scatter_sum_by_shifts(input_terms, "col", n_col, 0).astype(BF16)
    return (layer_out, input_grad, gate_wgrad, up_wgrad, down_wgrad)


def solution(mesh):
    n_dp, n_row, n_col = (mesh.shape[a] for a in ("dp", "row", "col"))
    devices = mesh.devices.reshape(n_dp, 2, n_row // 2, n_col)
    split = jax.sharding.Mesh(devices, ("dp", "rh", "rx", "col"))
    row = ("rh", "rx")
    in_specs = (
        P("dp", row + ("col",)),
        P("dp", row + ("col",)),
        P(row, "col"),
        P(row, "col"),
        P("col", row),
    )
    out_specs = (
        P(("dp", "col"), row),
        P(("dp", "col"), row),
        P(row, "col"),
        P(row, "col"),
        P("col", row),
    )
    return jax.shard_map(local, mesh=split, in_specs=in_specs, out_specs=out_specs, check_vma=False)
```

```python
import jax
import jax.numpy as jnp
from jax import lax
from jax.sharding import PartitionSpec as P

F32 = jnp.float32
BF16 = jnp.bfloat16


def contract_rows(left, right):
    return lax.dot_general(
        left, right, (((0,), (0,)), ((), ())), preferred_element_type=F32
    )


def contract_cols(left, right):
    return lax.dot_general(
        left, right, (((1,), (1,)), ((), ())), preferred_element_type=F32
    )


def shift_pairs(n, s):
    return [(i, (i + s) % n) for i in range(n)]


def gather_by_shifts(x, name, n, axis):
    me = lax.axis_index(name)
    blocks = [x]
    for t in range(1, n):
        blocks.append(lax.ppermute(x, name, shift_pairs(n, n - t)))
    doubled = jnp.concatenate(blocks + blocks, axis=axis)
    width = x.shape[axis]
    return lax.dynamic_slice_in_dim(doubled, (n - me) * width, n * width, axis=axis)


def scatter_sum_by_shifts(p, name, n, axis):
    me = lax.axis_index(name)
    width = p.shape[axis] // n
    acc = lax.dynamic_slice_in_dim(p, me * width, width, axis=axis).astype(F32)
    for s in range(1, n):
        block = lax.dynamic_slice_in_dim(p, ((me + s) % n) * width, width, axis=axis)
        acc = acc + lax.ppermute(block, name, shift_pairs(n, s)).astype(F32)
    return acc


def dp_allreduce(g):
    name = "dp"
    d = lax.axis_index(name)
    core = d % 2
    chip = d // 2
    to_core = [(i, i ^ 1) for i in range(4)]
    to_chip = [(i, i ^ 2) for i in range(4)]
    half = g.shape[0] // 2
    quarter = half // 2
    keep = lax.dynamic_slice_in_dim(g, core * half, half, 0)
    give = lax.dynamic_slice_in_dim(g, (1 - core) * half, half, 0)
    s1 = (keep.astype(F32) + lax.ppermute(give, name, to_core).astype(F32)).astype(BF16)
    keep2 = lax.dynamic_slice_in_dim(s1, chip * quarter, quarter, 0)
    give2 = lax.dynamic_slice_in_dim(s1, (1 - chip) * quarter, quarter, 0)
    s2 = (keep2.astype(F32) + lax.ppermute(give2, name, to_chip).astype(F32)).astype(BF16)
    other2 = lax.ppermute(s2, name, to_chip)
    mine_half = jnp.where(chip == 0, jnp.concatenate([s2, other2], 0), jnp.concatenate([other2, s2], 0))
    other_half = lax.ppermute(mine_half, name, to_core)
    return jnp.where(core == 0, jnp.concatenate([mine_half, other_half], 0),
                     jnp.concatenate([other_half, mine_half], 0))


def row_scatter_sum(p):
    n_x = 4
    rows, cols = p.shape
    blk = rows // (2 * n_x)
    s1 = scatter_sum_by_shifts(p.reshape(2, n_x * blk, cols), "rx", n_x, 1).astype(BF16)
    h = lax.axis_index("rh")
    keep = lax.dynamic_index_in_dim(s1, h, 0, keepdims=False)
    give = lax.dynamic_index_in_dim(s1, 1 - h, 0, keepdims=False)
    return keep.astype(F32) + lax.ppermute(give, "rh", [(0, 1), (1, 0)]).astype(F32)


def row_gather(v):
    n_x = 4
    h = lax.axis_index("rh")
    other = lax.ppermute(v, "rh", [(0, 1), (1, 0)])
    pair = jnp.where(h == 0, jnp.stack([v, other]), jnp.stack([other, v]))
    got = gather_by_shifts(pair, "rx", n_x, 1)
    return got.reshape(2 * n_x * v.shape[0], v.shape[1])


def local(tokens, cotangent, gate_weight, up_weight, down_weight):
    n_col = 8
    row = ("rh", "rx")
    whole_xt = lax.all_gather(tokens.T, "col", axis=0, tiled=True)
    whole_dy = gather_by_shifts(cotangent, "col", n_col, 1)
    gate = lax.psum_scatter(
        contract_rows(whole_xt, gate_weight).astype(BF16), row, scatter_dimension=0, tiled=True
    ).astype(F32)
    up = row_scatter_sum(contract_rows(whole_xt, up_weight).astype(BF16))
    hidden_grad = row_scatter_sum(contract_cols(whole_dy, down_weight).astype(BF16))
    sigma = jax.nn.sigmoid(gate)
    silu_gate = gate * sigma
    hidden = (silu_gate * up).astype(BF16)
    hidden_all = lax.all_gather(hidden, row, axis=0, tiled=True)
    out_terms = jnp.dot(hidden_all, down_weight, preferred_element_type=F32)
    layer_out = lax.psum_scatter(out_terms.astype(BF16), "col", scatter_dimension=0, tiled=True)
    down_part = contract_rows(hidden_all, whole_dy).astype(BF16)
    down_wgrad = dp_allreduce(down_part)
    gate_grad = (hidden_grad * up * sigma * (1.0 + gate * (1.0 - sigma))).astype(BF16)
    up_grad = (hidden_grad * silu_gate).astype(BF16)
    gate_all = row_gather(gate_grad)
    up_all = row_gather(up_grad)
    input_terms = (contract_cols(gate_all, gate_weight) + contract_cols(up_all, up_weight)).astype(BF16)
    input_grad = lax.psum_scatter(input_terms, "col", scatter_dimension=0, tiled=True)
    gate_part = jnp.dot(whole_xt, gate_all, preferred_element_type=F32).astype(BF16)
    up_part = jnp.dot(whole_xt, up_all, preferred_element_type=F32).astype(BF16)
    both_wgrad = dp_allreduce(jnp.concatenate([gate_part, up_part], axis=1))
    width = gate_part.shape[1]
    gate_wgrad = both_wgrad[:, :width]
    up_wgrad = both_wgrad[:, width:]
    return (layer_out, input_grad, gate_wgrad, up_wgrad, down_wgrad)


def solution(mesh):
    n_dp, n_row, n_col = (mesh.shape[a] for a in ("dp", "row", "col"))
    devices = mesh.devices.reshape(n_dp, 2, n_row // 2, n_col)
    split = jax.sharding.Mesh(devices, ("dp", "rh", "rx", "col"))
    row = ("rh", "rx")
    in_specs = (
        P("dp", row + ("col",)),
        P("dp", row + ("col",)),
        P(row, "col"),
        P(row, "col"),
        P("col", row),
    )
    out_specs = (
        P(("dp", "col"), row),
        P(("dp", "col"), row),
        P(row, "col"),
        P(row, "col"),
        P("col", row),
    )
    return jax.shard_map(local, mesh=split, in_specs=in_specs, out_specs=out_specs, check_vma=False)
```

```python
import jax
import jax.numpy as jnp
from jax import lax
from jax.sharding import PartitionSpec as P


F32 = jnp.float32
BF16 = jnp.bfloat16


def contract_rows(left, right):
    return lax.dot_general(
        left, right, (((0,), (0,)), ((), ())), preferred_element_type=F32
    )


def contract_cols(left, right):
    return lax.dot_general(
        left, right, (((1,), (1,)), ((), ())), preferred_element_type=F32
    )


def shift_pairs(n, s):
    return [(i, (i + s) % n) for i in range(n)]


def gather_by_shifts(x, name, n, axis):
    me = lax.axis_index(name)
    blocks = [x]
    for t in range(1, n):
        blocks.append(lax.ppermute(x, name, shift_pairs(n, n - t)))
    doubled = jnp.concatenate(blocks + blocks, axis=axis)
    width = x.shape[axis]
    return lax.dynamic_slice_in_dim(doubled, (n - me) * width, n * width, axis=axis)


def scatter_sum_by_shifts(p, name, n, axis):
    me = lax.axis_index(name)
    width = p.shape[axis] // n
    acc = lax.dynamic_slice_in_dim(p, me * width, width, axis=axis).astype(F32)
    for s in range(1, n):
        block = lax.dynamic_slice_in_dim(p, ((me + s) % n) * width, width, axis=axis)
        acc = acc + lax.ppermute(block, name, shift_pairs(n, s)).astype(F32)
    return acc


def dp_allreduce(g):
    name = "dp"
    d = lax.axis_index(name)
    core = d % 2
    chip = d // 2
    to_core = [(i, i ^ 1) for i in range(4)]
    to_chip = [(i, i ^ 2) for i in range(4)]
    half = g.shape[0] // 2
    quarter = half // 2
    keep = lax.dynamic_slice_in_dim(g, core * half, half, 0)
    give = lax.dynamic_slice_in_dim(g, (1 - core) * half, half, 0)
    s1 = (keep.astype(F32) + lax.ppermute(give, name, to_core).astype(F32)).astype(BF16)
    keep2 = lax.dynamic_slice_in_dim(s1, chip * quarter, quarter, 0)
    give2 = lax.dynamic_slice_in_dim(s1, (1 - chip) * quarter, quarter, 0)
    s2 = (keep2.astype(F32) + lax.ppermute(give2, name, to_chip).astype(F32)).astype(BF16)
    other2 = lax.ppermute(s2, name, to_chip)
    mine_half = jnp.where(chip == 0, jnp.concatenate([s2, other2], 0), jnp.concatenate([other2, s2], 0))
    other_half = lax.ppermute(mine_half, name, to_core)
    return jnp.where(core == 0, jnp.concatenate([mine_half, other_half], 0),
                     jnp.concatenate([other_half, mine_half], 0))


def row_scatter_sum(p):
    n_x = 4
    rows, cols = p.shape
    blk = rows // (2 * n_x)
    s1 = scatter_sum_by_shifts(p.reshape(2, n_x * blk, cols), "rx", n_x, 1).astype(BF16)
    h = lax.axis_index("rh")
    keep = lax.dynamic_index_in_dim(s1, h, 0, keepdims=False)
    give = lax.dynamic_index_in_dim(s1, 1 - h, 0, keepdims=False)
    return keep.astype(F32) + lax.ppermute(give, "rh", [(0, 1), (1, 0)]).astype(F32)


def row_gather(v):
    n_x = 4
    h = lax.axis_index("rh")
    other = lax.ppermute(v, "rh", [(0, 1), (1, 0)])
    pair = jnp.where(h == 0, jnp.stack([v, other]), jnp.stack([other, v]))
    got = gather_by_shifts(pair, "rx", n_x, 1)
    return got.reshape(2 * n_x * v.shape[0], v.shape[1])


def local_body(tokens, cotangent, gate_weight, up_weight, down_weight):
    n_col = 8
    row = ("rh", "rx")
    whole_xt = lax.all_gather(tokens.T, "col", axis=0, tiled=True)
    whole_dy = gather_by_shifts(cotangent, "col", n_col, 1)
    gate = lax.psum_scatter(
        contract_rows(whole_xt, gate_weight).astype(BF16), row, scatter_dimension=0, tiled=True
    ).astype(F32)
    up = row_scatter_sum(contract_rows(whole_xt, up_weight).astype(BF16))
    hidden_grad = row_scatter_sum(contract_cols(whole_dy, down_weight).astype(BF16))
    sigma = jax.nn.sigmoid(gate)
    silu_gate = gate * sigma
    hidden = (silu_gate * up).astype(BF16)
    hidden_all = lax.all_gather(hidden, row, axis=0, tiled=True)
    out_terms = jnp.dot(hidden_all, down_weight, preferred_element_type=F32).astype(BF16)
    down_part = contract_rows(hidden_all, whole_dy).astype(BF16)
    layer_out = lax.psum_scatter(out_terms, "col", scatter_dimension=0, tiled=True)
    down_wgrad = dp_allreduce(down_part)
    gate_grad = (hidden_grad * up * sigma * (1.0 + gate * (1.0 - sigma))).astype(BF16)
    up_grad = (hidden_grad * silu_gate).astype(BF16)
    gate_all = row_gather(gate_grad)
    up_all = row_gather(up_grad)
    input_terms = (contract_cols(gate_all, gate_weight) + contract_cols(up_all, up_weight)).astype(BF16)
    input_grad = lax.psum_scatter(input_terms, "col", scatter_dimension=0, tiled=True)
    gate_part = jnp.dot(whole_xt, gate_all, preferred_element_type=F32).astype(BF16)
    up_part = jnp.dot(whole_xt, up_all, preferred_element_type=F32).astype(BF16)
    both_wgrad = dp_allreduce(jnp.concatenate([gate_part, up_part], axis=1))
    width = gate_part.shape[1]
    gate_wgrad = both_wgrad[:, :width]
    up_wgrad = both_wgrad[:, width:]
    return (layer_out, input_grad, gate_wgrad, up_wgrad, down_wgrad)


def solution(mesh):
    n_dp, n_row, n_col = (mesh.shape[a] for a in ("dp", "row", "col"))
    devices = mesh.devices.reshape(n_dp, 2, n_row // 2, n_col)
    split = jax.sharding.Mesh(devices, ("dp", "rh", "rx", "col"))
    row = ("rh", "rx")
    in_specs = (
        P("dp", row + ("col",)),
        P("dp", row + ("col",)),
        P(row, "col"),
        P(row, "col"),
        P("col", row),
    )
    out_specs = (
        P(("dp", "col"), row),
        P(("dp", "col"), row),
        P(row, "col"),
        P(row, "col"),
        P("col", row),
    )
    return jax.shard_map(local_body, mesh=split, in_specs=in_specs, out_specs=out_specs, check_vma=False)
```

```python
import jax
import jax.numpy as jnp
from jax import lax
from jax.sharding import PartitionSpec as P


F32 = jnp.float32
BF16 = jnp.bfloat16


def contract_rows(left, right):
    return lax.dot_general(
        left, right, (((0,), (0,)), ((), ())), preferred_element_type=F32
    )


def contract_cols(left, right):
    return lax.dot_general(
        left, right, (((1,), (1,)), ((), ())), preferred_element_type=F32
    )


def shift_pairs(n, s):
    return [(i, (i + s) % n) for i in range(n)]


def gather_by_shifts(x, name, n, axis):
    me = lax.axis_index(name)
    blocks = [x]
    for t in range(1, n):
        blocks.append(lax.ppermute(x, name, shift_pairs(n, n - t)))
    doubled = jnp.concatenate(blocks + blocks, axis=axis)
    width = x.shape[axis]
    return lax.dynamic_slice_in_dim(doubled, (n - me) * width, n * width, axis=axis)


def scatter_sum_by_shifts(p, name, n, axis):
    me = lax.axis_index(name)
    width = p.shape[axis] // n
    acc = lax.dynamic_slice_in_dim(p, me * width, width, axis=axis).astype(F32)
    for s in range(1, n):
        block = lax.dynamic_slice_in_dim(p, ((me + s) % n) * width, width, axis=axis)
        acc = acc + lax.ppermute(block, name, shift_pairs(n, s)).astype(F32)
    return acc


def dp_allreduce(g):
    name = "dp"
    d = lax.axis_index(name)
    core = d % 2
    chip = d // 2
    to_core = [(i, i ^ 1) for i in range(4)]
    to_chip = [(i, i ^ 2) for i in range(4)]
    half = g.shape[0] // 2
    quarter = half // 2
    keep = lax.dynamic_slice_in_dim(g, core * half, half, 0)
    give = lax.dynamic_slice_in_dim(g, (1 - core) * half, half, 0)
    s1 = (keep.astype(F32) + lax.ppermute(give, name, to_core).astype(F32)).astype(BF16)
    keep2 = lax.dynamic_slice_in_dim(s1, chip * quarter, quarter, 0)
    give2 = lax.dynamic_slice_in_dim(s1, (1 - chip) * quarter, quarter, 0)
    s2 = (keep2.astype(F32) + lax.ppermute(give2, name, to_chip).astype(F32)).astype(BF16)
    other2 = lax.ppermute(s2, name, to_chip)
    mine_half = jnp.where(chip == 0, jnp.concatenate([s2, other2], 0), jnp.concatenate([other2, s2], 0))
    other_half = lax.ppermute(mine_half, name, to_core)
    return jnp.where(core == 0, jnp.concatenate([mine_half, other_half], 0),
                     jnp.concatenate([other_half, mine_half], 0))


def row_scatter_sum(p):
    n_x = 4
    rows, cols = p.shape
    blk = rows // (2 * n_x)
    s1 = scatter_sum_by_shifts(p.reshape(2, n_x * blk, cols), "rx", n_x, 1).astype(BF16)
    h = lax.axis_index("rh")
    keep = lax.dynamic_index_in_dim(s1, h, 0, keepdims=False)
    give = lax.dynamic_index_in_dim(s1, 1 - h, 0, keepdims=False)
    return keep.astype(F32) + lax.ppermute(give, "rh", [(0, 1), (1, 0)]).astype(F32)


def row_gather(v):
    n_x = 4
    h = lax.axis_index("rh")
    other = lax.ppermute(v, "rh", [(0, 1), (1, 0)])
    pair = jnp.where(h == 0, jnp.stack([v, other]), jnp.stack([other, v]))
    got = gather_by_shifts(pair, "rx", n_x, 1)
    return got.reshape(2 * n_x * v.shape[0], v.shape[1])


def local_body(tokens, cotangent, gate_weight, up_weight, down_weight):
    n_col = 8
    row = ("rh", "rx")
    whole_xt = lax.all_gather(tokens.T, "col", axis=0, tiled=True)
    whole_dy = gather_by_shifts(cotangent, "col", n_col, 1)
    gate = lax.psum_scatter(
        contract_rows(whole_xt, gate_weight).astype(BF16), row, scatter_dimension=0, tiled=True
    ).astype(F32)
    up = row_scatter_sum(contract_rows(whole_xt, up_weight).astype(BF16))
    hidden_grad = row_scatter_sum(contract_cols(whole_dy, down_weight).astype(BF16))
    sigma = jax.nn.sigmoid(gate)
    silu_gate = gate * sigma
    hidden = (silu_gate * up).astype(BF16)
    hidden_all = lax.all_gather(hidden, row, axis=0, tiled=True)
    out_terms = jnp.dot(hidden_all, down_weight, preferred_element_type=F32).astype(BF16)
    down_part = contract_rows(hidden_all, whole_dy).astype(BF16)
    layer_out = lax.psum_scatter(out_terms, "col", scatter_dimension=0, tiled=True)
    down_wgrad = dp_allreduce(down_part)
    gate_grad = (hidden_grad * up * sigma * (1.0 + gate * (1.0 - sigma))).astype(BF16)
    up_grad = (hidden_grad * silu_gate).astype(BF16)
    gate_all = row_gather(gate_grad)
    up_all = row_gather(up_grad)
    gate_part = jnp.dot(whole_xt, gate_all, preferred_element_type=F32).astype(BF16)
    gate_wgrad = dp_allreduce(gate_part)
    up_part = jnp.dot(whole_xt, up_all, preferred_element_type=F32).astype(BF16)
    up_wgrad = dp_allreduce(up_part)
    input_terms = (contract_cols(gate_all, gate_weight) + contract_cols(up_all, up_weight)).astype(BF16)
    input_grad = scatter_sum_by_shifts(input_terms, "col", n_col, 0).astype(BF16)
    return (layer_out, input_grad, gate_wgrad, up_wgrad, down_wgrad)


def solution(mesh):
    n_dp, n_row, n_col = (mesh.shape[a] for a in ("dp", "row", "col"))
    devices = mesh.devices.reshape(n_dp, 2, n_row // 2, n_col)
    split = jax.sharding.Mesh(devices, ("dp", "rh", "rx", "col"))
    row = ("rh", "rx")
    in_specs = (
        P("dp", row + ("col",)),
        P("dp", row + ("col",)),
        P(row, "col"),
        P(row, "col"),
        P("col", row),
    )
    out_specs = (
        P(("dp", "col"), row),
        P(("dp", "col"), row),
        P(row, "col"),
        P(row, "col"),
        P("col", row),
    )
    return jax.shard_map(local_body, mesh=split, in_specs=in_specs, out_specs=out_specs, check_vma=False)
```

```python
import jax
import jax.numpy as jnp
from jax import lax
from jax.sharding import PartitionSpec as P

F32 = jnp.float32
BF16 = jnp.bfloat16


def contract_rows(left, right):
    return lax.dot_general(
        left, right, (((0,), (0,)), ((), ())), preferred_element_type=F32
    )


def contract_cols(left, right):
    return lax.dot_general(
        left, right, (((1,), (1,)), ((), ())), preferred_element_type=F32
    )


def shift_pairs(n, s):
    return [(i, (i + s) % n) for i in range(n)]


def gather_by_shifts(x, name, n, axis):
    me = lax.axis_index(name)
    blocks = [x]
    for t in range(1, n):
        blocks.append(lax.ppermute(x, name, shift_pairs(n, n - t)))
    doubled = jnp.concatenate(blocks + blocks, axis=axis)
    width = x.shape[axis]
    return lax.dynamic_slice_in_dim(doubled, (n - me) * width, n * width, axis=axis)


def scatter_sum_by_shifts(p, name, n, axis):
    me = lax.axis_index(name)
    width = p.shape[axis] // n
    acc = lax.dynamic_slice_in_dim(p, me * width, width, axis=axis).astype(F32)
    for s in range(1, n):
        block = lax.dynamic_slice_in_dim(p, ((me + s) % n) * width, width, axis=axis)
        acc = acc + lax.ppermute(block, name, shift_pairs(n, s)).astype(F32)
    return acc


def dp_allreduce(g):
    name = "dp"
    d = lax.axis_index(name)
    core = d % 2
    chip = d // 2
    to_core = [(i, i ^ 1) for i in range(4)]
    to_chip = [(i, i ^ 2) for i in range(4)]
    half = g.shape[0] // 2
    quarter = half // 2
    keep = lax.dynamic_slice_in_dim(g, core * half, half, 0)
    give = lax.dynamic_slice_in_dim(g, (1 - core) * half, half, 0)
    s1 = (keep.astype(F32) + lax.ppermute(give, name, to_core).astype(F32)).astype(BF16)
    keep2 = lax.dynamic_slice_in_dim(s1, chip * quarter, quarter, 0)
    give2 = lax.dynamic_slice_in_dim(s1, (1 - chip) * quarter, quarter, 0)
    s2 = (keep2.astype(F32) + lax.ppermute(give2, name, to_chip).astype(F32)).astype(BF16)
    other2 = lax.ppermute(s2, name, to_chip)
    mine_half = lax.dynamic_update_slice_in_dim(
        jnp.concatenate([other2, other2], 0), s2, chip * quarter, 0)
    other_half = lax.ppermute(mine_half, name, to_core)
    return lax.dynamic_update_slice_in_dim(
        jnp.concatenate([other_half, other_half], 0), mine_half, core * half, 0)


def row_scatter_sum(p):
    n_x = 4
    rows, cols = p.shape
    blk = rows // (2 * n_x)
    s1 = scatter_sum_by_shifts(p.reshape(2, n_x * blk, cols), "rx", n_x, 1).astype(BF16)
    h = lax.axis_index("rh")
    keep = lax.dynamic_index_in_dim(s1, h, 0, keepdims=False)
    give = lax.dynamic_index_in_dim(s1, 1 - h, 0, keepdims=False)
    return keep.astype(F32) + lax.ppermute(give, "rh", [(0, 1), (1, 0)]).astype(F32)


def row_gather(v):
    n_x = 4
    h = lax.axis_index("rh")
    other = lax.ppermute(v, "rh", [(0, 1), (1, 0)])
    pair = jnp.where(h == 0, jnp.stack([v, other]), jnp.stack([other, v]))
    got = gather_by_shifts(pair, "rx", n_x, 1)
    return got.reshape(2 * n_x * v.shape[0], v.shape[1])


def local(tokens, cotangent, gate_weight, up_weight, down_weight):
    n_col = 8
    row = ("rh", "rx")
    whole_xt = lax.all_gather(tokens.T, "col", axis=0, tiled=True)
    whole_dy = gather_by_shifts(cotangent, "col", n_col, 1)
    gate = lax.psum_scatter(
        contract_rows(whole_xt, gate_weight).astype(BF16), row, scatter_dimension=0, tiled=True
    ).astype(F32)
    up = row_scatter_sum(contract_rows(whole_xt, up_weight).astype(BF16))
    hidden_grad = row_scatter_sum(contract_cols(whole_dy, down_weight).astype(BF16))
    sigma = jax.nn.sigmoid(gate)
    silu_gate = gate * sigma
    hidden = (silu_gate * up).astype(BF16)
    hidden_all = lax.all_gather(hidden, row, axis=0, tiled=True)
    out_terms = jnp.dot(hidden_all, down_weight, preferred_element_type=F32)
    layer_out = lax.psum_scatter(out_terms.astype(BF16), "col", scatter_dimension=0, tiled=True)
    down_part = contract_rows(hidden_all, whole_dy).astype(BF16)
    down_wgrad = dp_allreduce(down_part)
    gate_grad = (hidden_grad * up * sigma * (1.0 + gate * (1.0 - sigma))).astype(BF16)
    up_grad = (hidden_grad * silu_gate).astype(BF16)
    gate_all = row_gather(gate_grad)
    up_all = row_gather(up_grad)
    gate_part = jnp.dot(whole_xt, gate_all, preferred_element_type=F32).astype(BF16)
    gate_wgrad = dp_allreduce(gate_part)
    up_part = jnp.dot(whole_xt, up_all, preferred_element_type=F32).astype(BF16)
    up_wgrad = dp_allreduce(up_part)
    input_terms = (contract_cols(gate_all, gate_weight) + contract_cols(up_all, up_weight)).astype(BF16)
    input_grad = scatter_sum_by_shifts(input_terms, "col", n_col, 0).astype(BF16)
    return (layer_out, input_grad, gate_wgrad, up_wgrad, down_wgrad)


def solution(mesh):
    n_dp, n_row, n_col = (mesh.shape[a] for a in ("dp", "row", "col"))
    devices = mesh.devices.reshape(n_dp, 2, n_row // 2, n_col)
    split = jax.sharding.Mesh(devices, ("dp", "rh", "rx", "col"))
    row = ("rh", "rx")
    in_specs = (
        P("dp", row + ("col",)),
        P("dp", row + ("col",)),
        P(row, "col"),
        P(row, "col"),
        P("col", row),
    )
    out_specs = (
        P(("dp", "col"), row),
        P(("dp", "col"), row),
        P(row, "col"),
        P(row, "col"),
        P("col", row),
    )
    return jax.shard_map(local, mesh=split, in_specs=in_specs, out_specs=out_specs, check_vma=False)
```
